128 devices in a mesh: row: 8 (over x, core), col: 16 (over z, y).
Axes of the slice: x: 4, y: 4, z: 4, core: 2. Of those that a mesh axis runs over, the one named last changes fastest.
Arguments:
- unit_factor: float32 [4, 1024, 2, 2048], P(None, 'row', None, 'col'), may hold values from -0.125 to 0.125
- pivot_inverse: float32 [4, 1024, 2, 2048], P(None, 'row', None, 'col')
- supernode: int32 [32], replicated, may hold values from 0 to 2, never falling along the last dimension, each value on 1 to 16 neighbouring positions
- row_bits: int32 [32, 2], replicated, may hold values 0 or 1
Outputs:
- inverse_blocks: float32 [4, 1024, 2, 2048], P(None, 'row', None, 'col')
The draws below stay inside these ranges and needn't reach their ends.
Inputs may be any that keep to these rules, and one draw needn't show every extreme that they name: The supernode index never decreases from one block to the next; each supernode has 1 to 16 blocks, one of them exactly 16.
All inputs are finite; a program needn't handle non-finite values.
Results may differ from the reference program's by a relative error of at most 0.0001.
Values sent between devices are 32-bit elements; how exact they have to be, the bound alone decides.
No kernel may reach another device: no remote copies, remote signals or barrier semaphores. Data moves between devices by JAX's collectives and lax.ppermute only.
A program may use at most 128 MiB of HBM per device.

```python
import math
import jax
import jax.numpy as jnp
import numpy as np
from jax import lax

BS = 128
BR_DEV = 4
SUPERNODES = 3
NB = 32
BC_DEV = 2
N_ROW = 8
N_COL = 16


def draw_pivot_inverse(key, part):
    whole = NB * BS
    first = jax.random.fold_in(key, 0)
    second = jax.random.fold_in(key, 1)
    fourth = jax.random.fold_in(key, 3)
    noise = jax.random.normal(first, (whole, whole), jnp.float32)
    other = jax.random.normal(fourth, (whole, whole), jnp.float32)
    offdiag = (noise + other) * (0.35 / math.sqrt(BS))
    diagonal = jax.random.uniform(second, (whole,), jnp.float32, 1.0, 2.0)
    matrix = offdiag + jnp.eye(whole, dtype=jnp.float32) * diagonal[None, :]
    return matrix.reshape(BR_DEV, N_ROW * BS, BC_DEV, N_COL * BS)


def with_ends(values, own_key, least, high):
    longest = values.shape.index(max(values.shape))
    spots = []
    for shift in (0, 1):
        where = [jax.random.randint(jax.random.fold_in(own_key, axis), (), 0, length) for axis, length in enumerate(values.shape)]
        where[longest] = (where[longest] + shift) % values.shape[longest]
        spots.append(tuple(where))
    return values.at[spots[0]].set(least).at[spots[1]].set(high)


def level_of(own_key, dims, cuts, smallest, high):
    def one(axis_at, shards_of):
        draws = jax.random.uniform(jax.random.fold_in(jax.random.fold_in(own_key, 6), axis_at), (shards_of,), jnp.float32, smallest / len(cuts), high / len(cuts))
        return jnp.repeat(jnp.exp(draws), dims[axis_at] // shards_of).reshape((-1,) + (1,) * (len(dims) - axis_at - 1))

    factor_of = one(*cuts[0])
    for cut in cuts[1:]:
        factor_of = factor_of * one(*cut)
    return factor_of


def split_up(amount, total, limit, skew):
    portions = [(1 << 20) // math.isqrt(rank ** skew) + 1 for rank in range(2, amount + 1)]
    surplus, counts = total - limit - (amount - 1), [1] * (amount - 1)
    while surplus > 0:
        movable = [i for i in range(amount - 1) if counts[i] < limit]
        pool, budget = sum([portions[i] for i in movable]), surplus
        for i in movable:
            extra = min(limit - counts[i], max(1, budget * portions[i] // pool), surplus)
            counts[i] = counts[i] + extra
            surplus = surplus - extra
    return np.array([limit] + counts)


def ragged_sizes(own_key, count, total, reach, slope):
    if count == 2:
        one = jax.random.randint(own_key, (), max(1, total - reach), min(reach, total - 1) + 1)
        return jnp.stack([one, total - one])
    lengths = jnp.asarray(split_up(count, total, reach, slope), jnp.int32)
    pairs = (count - 1) // 2
    giver, taker = lengths[1:1 + 2 * pairs:2], lengths[2:2 + 2 * pairs:2]
    room = jnp.minimum(giver - 1, reach - taker)
    passed = jax.random.randint(jax.random.fold_in(own_key, 1), (pairs,), 0, 1 << 20) % (room + 1)
    lengths = lengths.at[1:1 + 2 * pairs:2].set(giver - passed).at[2:2 + 2 * pairs:2].set(taker + passed)
    return lengths[jax.random.permutation(jax.random.fold_in(own_key, 2), count)]


def normal_values(own_key, extent, width, bound, cuts=(), kind=jnp.bfloat16):
    level = level_of(own_key, extent, cuts, -0.22, 0.18) if cuts else 1.0
    array = jax.random.normal(own_key, extent, jnp.float32) * width * level
    return jnp.minimum(jnp.maximum(array, -bound), bound).astype(kind)


def setup_inputs(seed: int = 0) -> dict:
    splits = jax.random.split(jax.random.key(seed), 5)
    return {
        "unit_factor": normal_values(splits[0], (BR_DEV, N_ROW * BS, BC_DEV, N_COL * BS), (NB * BS // 2) ** -0.5, 0.125, ((1, 8), (3, 16)), jnp.float32),
        "pivot_inverse": draw_pivot_inverse(jax.random.fold_in(splits[4], 71), 0),
        "supernode": jnp.searchsorted(jnp.cumsum(ragged_sizes(splits[2], SUPERNODES, NB, NB // 2, 2)), jnp.arange(NB), side="right").astype(jnp.int32),
        "row_bits": with_ends((jax.random.randint(splits[3], (NB, SUPERNODES - 1), 0, 5) < 4).astype(jnp.int32), jax.random.fold_in(splits[3], 1), 0, 1),
    }


def reference(unit_factor, pivot_inverse, supernode, row_bits):
    whole = NB * BS
    factor = unit_factor.reshape(whole, whole)
    pivots = pivot_inverse.reshape(whole, whole)
    current = jnp.zeros((whole, whole), jnp.float32)
    for level in range(SUPERNODES - 1, -1, -1):
        member = jnp.repeat((supernode == level).astype(jnp.float32), BS)
        if level == SUPERNODES - 1:
            struct = jnp.zeros((whole,), jnp.float32)
        else:
            inside = jnp.logical_and(supernode > level, jnp.all(row_bits[:, level:] == 1, axis=1))
            struct = jnp.repeat(inside.astype(jnp.float32), BS)
        ancestors = current * struct[:, None] * struct[None, :]
        masked = factor * struct[:, None] * member[None, :]
        image = jnp.dot(ancestors, masked, precision=lax.Precision.HIGHEST, preferred_element_type=jnp.float32)
        update = jnp.dot(masked.T, image - ancestors, precision=lax.Precision.HIGHEST, preferred_element_type=jnp.float32)
        current = current - image + update + pivots * member[:, None] * member[None, :]
    return current.reshape(unit_factor.shape)
```

```python
import jax
import jax.numpy as jnp
from jax import lax
from jax.sharding import PartitionSpec as P

SUPERNODES = 3
HIGHEST = lax.Precision.HIGHEST


def dot(spec, a, b):
    return jnp.einsum(spec, a, b, precision=HIGHEST, preferred_element_type=jnp.float32)


def shards(unit_factor, pivot_inverse, supernode, row_bits):
    n_row = lax.axis_size("row")
    n_col = lax.axis_size("col")
    brows, width, bcols, _ = unit_factor.shape
    nb = brows * n_row
    r = lax.axis_index("row")
    q = lax.axis_index("col")

    def rows_of(v):
        return lax.dynamic_index_in_dim(v.reshape(brows, n_row), r, axis=1, keepdims=False)

    def cols_of(v):
        return lax.dynamic_index_in_dim(v.reshape(bcols, n_col), q, axis=1, keepdims=False)

    def mask(a, rm=None, cm=None):
        if rm is not None:
            a = a * rm[:, None, None, None]
        if cm is not None:
            a = a * cm[None, None, :, None]
        return a

    def pack_rows(a):
        return a.reshape((brows // 2, 2) + a.shape[1:]).sum(axis=0)

    def unpack_rows(a, rm):
        full = jnp.concatenate([a] * (brows // 2), axis=0)
        return full * rm.reshape((brows,) + (1,) * (a.ndim - 1))

    def scatter_rows(zp):
        zp = jnp.swapaxes(zp.reshape(n_col // n_row, n_row, width, bcols * width), 0, 1)
        zp = zp.reshape(n_col * width, bcols * width)
        zr = lax.psum_scatter(zp, "row", scatter_dimension=0, tiled=True)
        return zr.reshape(n_col // n_row, width, bcols, width)

    f32 = jnp.float32
    member = [(supernode == s).astype(f32) for s in range(SUPERNODES)]
    struct = [
        jnp.logical_and(supernode > s, jnp.all(row_bits[:, s:] == 1, axis=1)).astype(f32)
        for s in range(SUPERNODES - 1)
    ]

    last = SUPERNODES - 1
    rM2, cM2 = rows_of(member[last]), cols_of(member[last])
    x = mask(pivot_inverse, rM2, cM2)

    S, M = struct[1], member[1]
    rS, cS, rM, cM = rows_of(S), cols_of(S), rows_of(M), cols_of(M)
    xm = mask(x, rS, cS)
    xc = pack_rows(xm.sum(axis=2))
    uc = pack_rows(mask(unit_factor, rS, cM).sum(axis=2))
    xg = lax.all_gather(xc, "col")
    ucol = lax.all_gather(uc, "row")
    urow = lax.all_gather(uc, "col")
    xfull = jnp.transpose(xg, (1, 2, 0, 3))[:, :, None] * S.reshape(bcols, n_col)[None, None, :, :, None]
    xfull = xfull.reshape(2, width, nb, width)
    ufull = jnp.concatenate([jnp.transpose(ucol, (1, 0, 2, 3))] * (brows // 2), axis=0)
    ufull = (ufull * S.reshape(brows, n_row)[:, :, None, None]).reshape(nb, width, width)
    y = dot("pakx,kxb->pab", xfull, ufull)
    yl = mask(unpack_rows(y, rS)[:, :, None, :], None, cM)
    x = x - yl
    wc = pack_rows(yl - xm)
    zp = dot("qpax,pacb->qxcb", urow, wc)
    x = x + unpack_rows(scatter_rows(zp), rM) + mask(pivot_inverse, rM, cM)

    S, M = struct[0], member[0]
    rS, cS, rM, cM = rows_of(S), cols_of(S), rows_of(M), cols_of(M)
    xm = mask(x, rS, cS)
    uc = mask(unit_factor, rS, cM).sum(axis=2)
    ucol = lax.all_gather(uc, "row")
    urow = lax.all_gather(uc, "col")
    xg = lax.all_gather(xm, "col")
    xfull = jnp.transpose(xg, (1, 2, 3, 0, 4)).reshape(brows, width, nb, width)
    ufull = jnp.transpose(ucol, (1, 0, 2, 3)).reshape(nb, width, width)
    y = dot("takx,kxb->tab", xfull, ufull)
    yl = mask(y[:, :, None, :], None, cM)
    x = x - yl
    zp = dot("qtax,tacb->qxcb", urow, yl - xm)
    x = x + unpack_rows(scatter_rows(zp), rM) + mask(pivot_inverse, rM, cM)
    return x


def solution(mesh):
    in_specs = (P(None, "row", None, "col"), P(None, "row", None, "col"), P(), P())
    out_specs = P(None, "row", None, "col")
    return jax.shard_map(shards, mesh=mesh, in_specs=in_specs, out_specs=out_specs, check_vma=False)
```

```python
import jax
import jax.numpy as jnp
from jax import lax
from jax.sharding import PartitionSpec as P

SUPERNODES = 3
HIGHEST = lax.Precision.HIGHEST


def dot(spec, a, b):
    return jnp.einsum(spec, a, b, precision=HIGHEST, preferred_element_type=jnp.float32)


def shards(unit_factor, pivot_inverse, supernode, row_bits):
    n_row = lax.axis_size("row")
    n_col = lax.axis_size("col")
    brows, width, bcols, _ = unit_factor.shape
    nb = brows * n_row
    r = lax.axis_index("row")
    q = lax.axis_index("col")

    def rows_of(v):
        return lax.dynamic_index_in_dim(v.reshape(brows, n_row), r, axis=1, keepdims=False)

    def cols_of(v):
        return lax.dynamic_index_in_dim(v.reshape(bcols, n_col), q, axis=1, keepdims=False)

    def mask(a, rm=None, cm=None):
        if rm is not None:
            a = a * rm[:, None, None, None]
        if cm is not None:
            a = a * cm[None, None, :, None]
        return a

    def pack_rows(a):
        return a.reshape((brows // 2, 2) + a.shape[1:]).sum(axis=0)

    def unpack_rows(a, rm):
        full = jnp.concatenate([a] * (brows // 2), axis=0)
        return full * rm.reshape((brows,) + (1,) * (a.ndim - 1))

    def scatter_rows(zp):
        zp = jnp.swapaxes(zp.reshape(n_col // n_row, n_row, width, bcols * width), 0, 1)
        zp = zp.reshape(n_col * width, bcols * width)
        zr = lax.psum_scatter(zp, "row", scatter_dimension=0, tiled=True)
        return zr.reshape(n_col // n_row, width, bcols, width)

    f32 = jnp.float32
    member = [(supernode == s).astype(f32) for s in range(SUPERNODES)]
    struct = [
        jnp.logical_and(supernode > s, jnp.all(row_bits[:, s:] == 1, axis=1)).astype(f32)
        for s in range(SUPERNODES - 1)
    ]

    last = SUPERNODES - 1
    rM2, cM2 = rows_of(member[last]), cols_of(member[last])
    x = mask(pivot_inverse, rM2, cM2)

    S1, M1, S0, M0 = struct[1], member[1], struct[0], member[0]
    rS1, cS1, rM1, cM1 = rows_of(S1), cols_of(S1), rows_of(M1), cols_of(M1)
    rS0, cS0, rM0, cM0 = rows_of(S0), cols_of(S0), rows_of(M0), cols_of(M0)

    xm = mask(x, rS1, cS1)
    xc1 = pack_rows(xm.sum(axis=2))
    uc1 = pack_rows(mask(unit_factor, rS1, cM1).sum(axis=2))
    uc0 = mask(unit_factor, rS0, cM0).sum(axis=2)
    gcol = lax.all_gather(jnp.concatenate([xc1, uc1, uc0], axis=0), "col")
    grow = lax.all_gather(jnp.concatenate([uc1, uc0], axis=0), "row")
    xg, urow1, urow0 = gcol[:, 0:2], gcol[:, 2:4], gcol[:, 4:8]
    ucol1, ucol0 = grow[:, 0:2], grow[:, 2:6]

    xfull = jnp.transpose(xg, (1, 2, 0, 3))[:, :, None] * S1.reshape(bcols, n_col)[None, None, :, :, None]
    xfull = xfull.reshape(2, width, nb, width)
    ufull = jnp.concatenate([jnp.transpose(ucol1, (1, 0, 2, 3))] * (brows // 2), axis=0)
    ufull = (ufull * S1.reshape(brows, n_row)[:, :, None, None]).reshape(nb, width, width)
    y = dot("pakx,kxb->pab", xfull, ufull)
    yl = mask(unpack_rows(y, rS1)[:, :, None, :], None, cM1)
    x = x - yl
    wc = pack_rows(yl - xm)
    zp = dot("qpax,pacb->qxcb", urow1, wc)
    x = x + unpack_rows(scatter_rows(zp), rM1) + mask(pivot_inverse, rM1, cM1)

    xm = mask(x, rS0, cS0)
    xg = lax.all_gather(xm, "col")
    xfull = jnp.transpose(xg, (1, 2, 3, 0, 4)).reshape(brows, width, nb, width)
    ufull = jnp.transpose(ucol0, (1, 0, 2, 3)).reshape(nb, width, width)
    y = dot("takx,kxb->tab", xfull, ufull)
    yl = mask(y[:, :, None, :], None, cM0)
    x = x - yl
    zp = dot("qtax,tacb->qxcb", urow0, yl - xm)
    x = x + unpack_rows(scatter_rows(zp), rM0) + mask(pivot_inverse, rM0, cM0)
    return x


def solution(mesh):
    in_specs = (P(None, "row", None, "col"), P(None, "row", None, "col"), P(), P())
    out_specs = P(None, "row", None, "col")
    return jax.shard_map(shards, mesh=mesh, in_specs=in_specs, out_specs=out_specs, check_vma=False)
```

```python
import jax
import jax.numpy as jnp
from jax import lax
from jax.sharding import PartitionSpec as P

SUPERNODES = 3
HIGHEST = lax.Precision.HIGHEST


def dot(spec, a, b):
    return jnp.einsum(spec, a, b, precision=HIGHEST, preferred_element_type=jnp.float32)


def shards(unit_factor, pivot_inverse, supernode, row_bits):
    n_row = lax.axis_size("row")
    n_col = lax.axis_size("col")
    brows, width, bcols, _ = unit_factor.shape
    nb = brows * n_row
    r = lax.axis_index("row")
    q = lax.axis_index("col")

    def rows_of(v):
        return lax.dynamic_index_in_dim(v.reshape(brows, n_row), r, axis=1, keepdims=False)

    def cols_of(v):
        return lax.dynamic_index_in_dim(v.reshape(bcols, n_col), q, axis=1, keepdims=False)

    def mask(a, rm=None, cm=None):
        if rm is not None:
            a = a * rm[:, None, None, None]
        if cm is not None:
            a = a * cm[None, None, :, None]
        return a

    def pack_rows(a):
        return a.reshape((brows // 2, 2) + a.shape[1:]).sum(axis=0)

    def unpack_rows(a, rm):
        full = jnp.concatenate([a] * (brows // 2), axis=0)
        return full * rm.reshape((brows,) + (1,) * (a.ndim - 1))

    def scatter_rows(zp):
        zp = jnp.swapaxes(zp.reshape(n_col // n_row, n_row, width, bcols * width), 0, 1)
        zp = zp.reshape(n_col * width, bcols * width)
        zr = lax.psum_scatter(zp, "row", scatter_dimension=0, tiled=True)
        return zr.reshape(n_col // n_row, width, bcols, width)

    f32 = jnp.float32
    member = [(supernode == s).astype(f32) for s in range(SUPERNODES)]
    struct = [
        jnp.logical_and(supernode > s, jnp.all(row_bits[:, s:] == 1, axis=1)).astype(f32)
        for s in range(SUPERNODES - 1)
    ]

    last = SUPERNODES - 1
    rM2, cM2 = rows_of(member[last]), cols_of(member[last])
    x = mask(pivot_inverse, rM2, cM2)

    S1, M1, S0, M0 = struct[1], member[1], struct[0], member[0]
    rS1, cS1, rM1, cM1 = rows_of(S1), cols_of(S1), rows_of(M1), cols_of(M1)
    rS0, cS0, rM0, cM0 = rows_of(S0), cols_of(S0), rows_of(M0), cols_of(M0)

    xm = mask(x, rS1, cS1)
    xc1 = pack_rows(xm.sum(axis=2))
    uc1 = pack_rows(mask(unit_factor, rS1, cM1).sum(axis=2))
    uc0 = mask(unit_factor, rS0, cM0).sum(axis=2)
    gcol = lax.all_gather(jnp.concatenate([xc1, uc1, uc0], axis=0), "col")
    send = jnp.concatenate([uc1, uc0], axis=0)
    pieces = [send] + [lax.ppermute(send, "row", [(i, (i + d) % n_row) for i in range(n_row)]) for d in range(1, n_row)]
    by_shift = jnp.stack(pieces)
    grow = jnp.take(by_shift, (r - jnp.arange(n_row)) % n_row, axis=0)
    xg, urow1, urow0 = gcol[:, 0:2], gcol[:, 2:4], gcol[:, 4:8]
    ucol1, ucol0 = grow[:, 0:2], grow[:, 2:6]

    xfull = jnp.transpose(xg, (1, 2, 0, 3))[:, :, None] * S1.reshape(bcols, n_col)[None, None, :, :, None]
    xfull = xfull.reshape(2, width, nb, width)
    ufull = jnp.concatenate([jnp.transpose(ucol1, (1, 0, 2, 3))] * (brows // 2), axis=0)
    ufull = (ufull * S1.reshape(brows, n_row)[:, :, None, None]).reshape(nb, width, width)
    y = dot("pakx,kxb->pab", xfull, ufull)
    yl = mask(unpack_rows(y, rS1)[:, :, None, :], None, cM1)
    x = x - yl
    wc = pack_rows(yl - xm)
    zp = dot("qpax,pacb->qxcb", urow1, wc)
    x = x + unpack_rows(scatter_rows(zp), rM1) + mask(pivot_inverse, rM1, cM1)

    xm = mask(x, rS0, cS0)
    xg = lax.all_gather(xm, "col")
    xfull = jnp.transpose(xg, (1, 2, 3, 0, 4)).reshape(brows, width, nb, width)
    ufull = jnp.transpose(ucol0, (1, 0, 2, 3)).reshape(nb, width, width)
    y = dot("takx,kxb->tab", xfull, ufull)
    yl = mask(y[:, :, None, :], None, cM0)
    x = x - yl
    zp = dot("qtax,tacb->qxcb", urow0, yl - xm)
    x = x + unpack_rows(scatter_rows(zp), rM0) + mask(pivot_inverse, rM0, cM0)
    return x


def solution(mesh):
    in_specs = (P(None, "row", None, "col"), P(None, "row", None, "col"), P(), P())
    out_specs = P(None, "row", None, "col")
    return jax.shard_map(shards, mesh=mesh, in_specs=in_specs, out_specs=out_specs, check_vma=False)
```

```python
import jax
import jax.numpy as jnp
from jax import lax
from jax.sharding import PartitionSpec as P


SUPERNODES = 3
HIGHEST = lax.Precision.HIGHEST
ROW_STAGES = ((1, 2), (2, 4))
COL_STAGES = ((1, 4), (4, 4))


def dot(spec, a, b):
    return jnp.einsum(spec, a, b, precision=HIGHEST, preferred_element_type=jnp.float32)


def pp_gather(a, axis, stages):
    n = lax.axis_size(axis)
    me = lax.axis_index(axis)
    out = a[None]
    for stride, count in stages:
        def to(i, d, stride=stride, count=count):
            digit = (i // stride) % count
            return i + (((digit + d) % count) - digit) * stride

        parts = [out] + [lax.ppermute(out, axis, [(i, to(i, d)) for i in range(n)]) for d in range(1, count)]
        out = jnp.concatenate(parts, axis=0)
    src = jnp.arange(n)
    at = jnp.zeros((n,), jnp.int32)
    mult = 1
    for stride, count in stages:
        at = at + ((me // stride - src // stride) % count) * mult
        mult *= count
    return jnp.take(out, at, axis=0)


def shards(unit_factor, pivot_inverse, supernode, row_bits):
    n_row = lax.axis_size("row")
    n_col = lax.axis_size("col")
    brows, width, bcols, _ = unit_factor.shape
    nb = brows * n_row
    r = lax.axis_index("row")
    q = lax.axis_index("col")

    def rows_of(v):
        return lax.dynamic_index_in_dim(v.reshape(brows, n_row), r, axis=1, keepdims=False)

    def cols_of(v):
        return lax.dynamic_index_in_dim(v.reshape(bcols, n_col), q, axis=1, keepdims=False)

    def mask(a, rm=None, cm=None):
        if rm is not None:
            a = a * rm[:, None, None, None]
        if cm is not None:
            a = a * cm[None, None, :, None]
        return a

    def pack_rows(a):
        return a.reshape((brows // 2, 2) + a.shape[1:]).sum(axis=0)

    def unpack_rows(a, rm):
        full = jnp.concatenate([a] * (brows // 2), axis=0)
        return full * rm.reshape((brows,) + (1,) * (a.ndim - 1))

    def scatter_rows(zp):
        zp = jnp.swapaxes(zp.reshape(n_col // n_row, n_row, width, bcols * width), 0, 1)
        zp = zp.reshape(n_col * width, bcols * width)
        zr = lax.psum_scatter(zp, "row", scatter_dimension=0, tiled=True)
        return zr.reshape(n_col // n_row, width, bcols, width)

    f32 = jnp.float32
    member = [(supernode == s).astype(f32) for s in range(SUPERNODES)]
    struct = [
        jnp.logical_and(supernode > s, jnp.all(row_bits[:, s:] == 1, axis=1)).astype(f32)
        for s in range(SUPERNODES - 1)
    ]

    last = SUPERNODES - 1
    rM2, cM2 = rows_of(member[last]), cols_of(member[last])
    x = mask(pivot_inverse, rM2, cM2)

    S1, M1, S0, M0 = struct[1], member[1], struct[0], member[0]
    rS1, cS1, rM1, cM1 = rows_of(S1), cols_of(S1), rows_of(M1), cols_of(M1)
    rS0, cS0, rM0, cM0 = rows_of(S0), cols_of(S0), rows_of(M0), cols_of(M0)

    xm = mask(x, rS1, cS1)
    xc1 = pack_rows(xm.sum(axis=2))
    uc1 = pack_rows(mask(unit_factor, rS1, cM1).sum(axis=2))
    uc0 = mask(unit_factor, rS0, cM0).sum(axis=2)
    gcol = lax.all_gather(jnp.concatenate([xc1, uc1, uc0], axis=0), "col")
    grow = pp_gather(jnp.concatenate([uc1, uc0], axis=0), "row", ROW_STAGES)
    xg, urow1, urow0 = gcol[:, 0:2], gcol[:, 2:4], gcol[:, 4:8]
    ucol1, ucol0 = grow[:, 0:2], grow[:, 2:6]

    xfull = jnp.transpose(xg, (1, 2, 0, 3))[:, :, None] * S1.reshape(bcols, n_col)[None, None, :, :, None]
    xfull = xfull.reshape(2, width, nb, width)
    ufull = jnp.concatenate([jnp.transpose(ucol1, (1, 0, 2, 3))] * (brows // 2), axis=0)
    ufull = (ufull * S1.reshape(brows, n_row)[:, :, None, None]).reshape(nb, width, width)
    y = dot("pakx,kxb->pab", xfull, ufull)
    yl = mask(unpack_rows(y, rS1)[:, :, None, :], None, cM1)
    x = x - yl
    wc = pack_rows(yl - xm)
    zp = dot("qpax,pacb->qxcb", urow1, wc)

    xm = mask(x, rS0, cS0)
    early, zp = lax.optimization_barrier((pack_rows(mask(xm, rM2)), zp))
    g_early = pp_gather(early, "col", COL_STAGES)
    z1 = scatter_rows(zp)
    x = x + unpack_rows(z1, rM1) + mask(pivot_inverse, rM1, cM1)
    xm = mask(x, rS0, cS0)
    late = pack_rows(mask(xm, rM1))
    g_late = lax.all_gather(late, "col")
    xg = jnp.concatenate([g_early, g_late], axis=1)
    xfull = jnp.transpose(xg, (1, 2, 3, 0, 4)).reshape(brows, width, nb, width)
    ufull = jnp.transpose(ucol0, (1, 0, 2, 3)).reshape(nb, width, width)
    y = dot("takx,kxb->tab", xfull, ufull)
    y = unpack_rows(y[0:2], rM2) + unpack_rows(y[2:4], rM1)
    yl = mask(y[:, :, None, :], None, cM0)
    x = x - yl
    zp = dot("qtax,tacb->qxcb", urow0, yl - xm)
    x = x + unpack_rows(scatter_rows(zp), rM0) + mask(pivot_inverse, rM0, cM0)
    return x


def solution(mesh):
    in_specs = (P(None, "row", None, "col"), P(None, "row", None, "col"), P(), P())
    out_specs = P(None, "row", None, "col")
    return jax.shard_map(shards, mesh=mesh, in_specs=in_specs, out_specs=out_specs, check_vma=False)
```

```python
import jax
import jax.numpy as jnp
from jax import lax
from jax.sharding import PartitionSpec as P

SUPERNODES = 3
HIGHEST = lax.Precision.HIGHEST
ROW_STAGES = ((1, 2), (2, 4))


def dot(spec, a, b):
    return jnp.einsum(spec, a, b, precision=HIGHEST, preferred_element_type=jnp.float32)


def pp_gather(a, axis, stages):
    n = lax.axis_size(axis)
    me = lax.axis_index(axis)
    out = a[None]
    for stride, count in stages:
        def to(i, d, stride=stride, count=count):
            digit = (i // stride) % count
            return i + (((digit + d) % count) - digit) * stride

        parts = [out] + [lax.ppermute(out, axis, [(i, to(i, d)) for i in range(n)]) for d in range(1, count)]
        out = jnp.concatenate(parts, axis=0)
    src = jnp.arange(n)
    at = jnp.zeros((n,), jnp.int32)
    mult = 1
    for stride, count in stages:
        at = at + ((me // stride - src // stride) % count) * mult
        mult *= count
    return jnp.take(out, at, axis=0)


def pp_scatter(parts, axis, stages):
    n = lax.axis_size(axis)
    me = lax.axis_index(axis)
    counts = [count for _, count in stages]
    acc = parts.reshape(tuple(reversed(counts)) + parts.shape[1:])
    for stride, count in reversed(stages):
        mine = (me // stride) % count

        def to(i, d, stride=stride, count=count):
            digit = (i // stride) % count
            return i + (((digit + d) % count) - digit) * stride

        total = jnp.take(acc, mine, axis=0)
        for d in range(1, count):
            piece = jnp.take(acc, (mine + d) % count, axis=0)
            total = total + lax.ppermute(piece, axis, [(i, to(i, d)) for i in range(n)])
        acc = total
    return acc


def pp_scatter_rows(zp, n_row, n_col, width, bcols):
    parts = jnp.swapaxes(zp.reshape((n_col // n_row, n_row) + zp.shape[1:]), 0, 1)
    return pp_scatter(parts, "row", ROW_STAGES)


def shards(unit_factor, pivot_inverse, supernode, row_bits):
    n_row = lax.axis_size("row")
    n_col = lax.axis_size("col")
    brows, width, bcols, _ = unit_factor.shape
    nb = brows * n_row
    r = lax.axis_index("row")
    q = lax.axis_index("col")

    def rows_of(v):
        return lax.dynamic_index_in_dim(v.reshape(brows, n_row), r, axis=1, keepdims=False)

    def cols_of(v):
        return lax.dynamic_index_in_dim(v.reshape(bcols, n_col), q, axis=1, keepdims=False)

    def mask(a, rm=None, cm=None):
        if rm is not None:
            a = a * rm[:, None, None, None]
        if cm is not None:
            a = a * cm[None, None, :, None]
        return a

    def pack_rows(a):
        return a.reshape((brows // 2, 2) + a.shape[1:]).sum(axis=0)

    def unpack_rows(a, rm):
        full = jnp.concatenate([a] * (brows // 2), axis=0)
        return full * rm.reshape((brows,) + (1,) * (a.ndim - 1))

    def scatter_rows(zp):
        tail = zp.shape[2:]
        zp = jnp.swapaxes(zp.reshape((n_col // n_row, n_row, width) + tail), 0, 1)
        zp = zp.reshape(n_col * width, -1)
        zr = lax.psum_scatter(zp, "row", scatter_dimension=0, tiled=True)
        return zr.reshape((n_col // n_row, width) + tail)

    f32 = jnp.float32
    member = [(supernode == s).astype(f32) for s in range(SUPERNODES)]
    struct = [
        jnp.logical_and(supernode > s, jnp.all(row_bits[:, s:] == 1, axis=1)).astype(f32)
        for s in range(SUPERNODES - 1)
    ]

    last = SUPERNODES - 1
    rM2, cM2 = rows_of(member[last]), cols_of(member[last])
    x = mask(pivot_inverse, rM2, cM2)

    S1, M1, S0, M0 = struct[1], member[1], struct[0], member[0]
    rS1, cS1, rM1, cM1 = rows_of(S1), cols_of(S1), rows_of(M1), cols_of(M1)
    rS0, cS0, rM0, cM0 = rows_of(S0), cols_of(S0), rows_of(M0), cols_of(M0)

    xm = mask(x, rS1, cS1)
    xc1 = pack_rows(xm.sum(axis=2))
    uc1 = pack_rows(mask(unit_factor, rS1, cM1).sum(axis=2))
    uc0 = mask(unit_factor, rS0, cM0).sum(axis=2)
    gcol = lax.all_gather(jnp.concatenate([xc1, uc1, uc0], axis=0), "col")
    grow = pp_gather(jnp.concatenate([uc1, uc0], axis=0), "row", ROW_STAGES)
    xg, urow1, urow0 = gcol[:, 0:2], gcol[:, 2:4], gcol[:, 4:8]
    ucol1, ucol0 = grow[:, 0:2], grow[:, 2:6]

    xfull = jnp.transpose(xg, (1, 2, 0, 3))[:, :, None] * S1.reshape(bcols, n_col)[None, None, :, :, None]
    xfull = xfull.reshape(2, width, nb, width)
    ufull = jnp.concatenate([jnp.transpose(ucol1, (1, 0, 2, 3))] * (brows // 2), axis=0)
    ufull = (ufull * S1.reshape(brows, n_row)[:, :, None, None]).reshape(nb, width, width)
    za = pp_scatter_rows(-dot("qpax,pacb->qxcb", urow1, pack_rows(xm)), n_row, n_col, width, bcols)
    y = dot("pakx,kxb->pab", xfull, ufull)
    yl = mask(unpack_rows(y, rS1)[:, :, None, :], None, cM1)
    x = x - yl
    zb = scatter_rows(dot("qpax,pab->qxb", urow1, y))
    z = za + zb[:, :, None, :] * cM1[None, None, :, None]
    x = x + unpack_rows(z, rM1) + mask(pivot_inverse, rM1, cM1)

    xm = mask(x, rS0, cS0)
    xg = lax.all_gather(xm, "col")
    xfull = jnp.transpose(xg, (1, 2, 3, 0, 4)).reshape(brows, width, nb, width)
    ufull = jnp.transpose(ucol0, (1, 0, 2, 3)).reshape(nb, width, width)
    za = pp_scatter_rows(-dot("qtax,tacb->qxcb", urow0, xm), n_row, n_col, width, bcols)
    y = dot("takx,kxb->tab", xfull, ufull)
    yl = mask(y[:, :, None, :], None, cM0)
    x = x - yl
    zb = scatter_rows(dot("qtax,tab->qxb", urow0, y))
    z = za + zb[:, :, None, :] * cM0[None, None, :, None]
    x = x + unpack_rows(z, rM0) + mask(pivot_inverse, rM0, cM0)
    return x


def solution(mesh):
    in_specs = (P(None, "row", None, "col"), P(None, "row", None, "col"), P(), P())
    out_specs = P(None, "row", None, "col")
    return jax.shard_map(shards, mesh=mesh, in_specs=in_specs, out_specs=out_specs, check_vma=False)
```

```python
import jax
import jax.numpy as jnp
from jax import lax
from jax.sharding import PartitionSpec as P

SUPERNODES = 3
HIGHEST = lax.Precision.HIGHEST


def dot(spec, a, b):
    return jnp.einsum(spec, a, b, precision=HIGHEST, preferred_element_type=jnp.float32)


def shards(unit_factor, pivot_inverse, supernode, row_bits):
    n_row = lax.axis_size("row")
    n_col = lax.axis_size("col")
    brows, width, bcols, _ = unit_factor.shape
    nb = brows * n_row
    r = lax.axis_index("row")
    q = lax.axis_index("col")

    def rows_of(v):
        return lax.dynamic_index_in_dim(v.reshape(brows, n_row), r, axis=1, keepdims=False)

    def cols_of(v):
        return lax.dynamic_index_in_dim(v.reshape(bcols, n_col), q, axis=1, keepdims=False)

    def mask(a, rm=None, cm=None):
        if rm is not None:
            a = a * rm[:, None, None, None]
        if cm is not None:
            a = a * cm[None, None, :, None]
        return a

    def pack_rows(a):
        return a.reshape((brows // 2, 2) + a.shape[1:]).sum(axis=0)

    def unpack_rows(a, rm):
        full = jnp.concatenate([a] * (brows // 2), axis=0)
        return full * rm.reshape((brows,) + (1,) * (a.ndim - 1))

    def scatter_rows(zp):
        zp = jnp.swapaxes(zp.reshape(n_col // n_row, n_row, width, bcols * width), 0, 1)
        zp = zp.reshape(n_col * width, bcols * width)
        zr = lax.psum_scatter(zp, "row", scatter_dimension=0, tiled=True)
        return zr.reshape(n_col // n_row, width, bcols, width)

    f32 = jnp.float32
    member = [(supernode == s).astype(f32) for s in range(SUPERNODES)]
    struct = [
        jnp.logical_and(supernode > s, jnp.all(row_bits[:, s:] == 1, axis=1)).astype(f32)
        for s in range(SUPERNODES - 1)
    ]

    last = SUPERNODES - 1
    rM2, cM2 = rows_of(member[last]), cols_of(member[last])
    x = mask(pivot_inverse, rM2, cM2)

    S1, M1, S0, M0 = struct[1], member[1], struct[0], member[0]
    rS1, cS1, rM1, cM1 = rows_of(S1), cols_of(S1), rows_of(M1), cols_of(M1)
    rS0, cS0, rM0, cM0 = rows_of(S0), cols_of(S0), rows_of(M0), cols_of(M0)

    xm = mask(x, rS1, cS1)
    xc1 = pack_rows(xm.sum(axis=2))
    uc1 = pack_rows(mask(unit_factor, rS1, cM1).sum(axis=2))
    uc0 = mask(unit_factor, rS0, cM0).sum(axis=2)
    gcol = lax.all_gather(jnp.concatenate([xc1, uc1, uc0], axis=0), "col")
    send = jnp.concatenate([uc1, uc0], axis=0)
    pieces = [send] + [lax.ppermute(send, "row", [(i, (i + d) % n_row) for i in range(n_row)]) for d in range(1, n_row)]
    by_shift = jnp.stack(pieces)
    grow = jnp.take(by_shift, (r - jnp.arange(n_row)) % n_row, axis=0)
    xg, urow1, urow0 = gcol[:, 0:2], gcol[:, 2:4], gcol[:, 4:8]
    ucol1, ucol0 = grow[:, 0:2], grow[:, 2:6]

    s1 = S1.reshape(bcols, n_col).sum(axis=0)
    ueff = jnp.transpose(ucol1, (1, 0, 2, 3)).reshape(n_col, width, width) * s1[:, None, None]
    y = dot("qpax,qxb->pab", xg, ueff)
    yl = mask(unpack_rows(y, rS1)[:, :, None, :], None, cM1)
    x = x - yl
    wc = pack_rows(yl - xm)
    zp = dot("qpax,pacb->qxcb", urow1, wc)
    x = x + unpack_rows(scatter_rows(zp), rM1) + mask(pivot_inverse, rM1, cM1)

    xm = mask(x, rS0, cS0)
    xg = lax.all_gather(xm, "col", axis=2)
    u2 = ucol0.reshape(n_row, bcols, n_col // n_row, width, width)
    u2 = jnp.transpose(u2, (2, 0, 1, 3, 4)).reshape(n_col, bcols, width, width)
    y = dot("taqcx,qcxb->tab", xg, u2)
    yl = mask(y[:, :, None, :], None, cM0)
    x = x - yl
    zp = dot("qtax,tacb->qxcb", urow0, yl - xm)
    x = x + unpack_rows(scatter_rows(zp), rM0) + mask(pivot_inverse, rM0, cM0)
    return x


def solution(mesh):
    in_specs = (P(None, "row", None, "col"), P(None, "row", None, "col"), P(), P())
    out_specs = P(None, "row", None, "col")
    return jax.shard_map(shards, mesh=mesh, in_specs=in_specs, out_specs=out_specs, check_vma=False)
```

```python
import jax
import jax.numpy as jnp
from jax import lax
from jax.sharding import PartitionSpec as P

SUPERNODES = 3
PRECISION = lax.Precision.HIGH


def dot(spec, a, b):
    return jnp.einsum(spec, a, b, precision=PRECISION, preferred_element_type=jnp.float32)


def shards(unit_factor, pivot_inverse, supernode, row_bits):
    n_row = lax.axis_size("row")
    n_col = lax.axis_size("col")
    brows, width, bcols, _ = unit_factor.shape
    nb = brows * n_row
    r = lax.axis_index("row")
    q = lax.axis_index("col")

    def rows_of(v):
        return lax.dynamic_index_in_dim(v.reshape(brows, n_row), r, axis=1, keepdims=False)

    def cols_of(v):
        return lax.dynamic_index_in_dim(v.reshape(bcols, n_col), q, axis=1, keepdims=False)

    def mask(a, rm=None, cm=None):
        if rm is not None:
            a = a * rm[:, None, None, None]
        if cm is not None:
            a = a * cm[None, None, :, None]
        return a

    def pack_rows(a):
        return a.reshape((brows // 2, 2) + a.shape[1:]).sum(axis=0)

    def unpack_rows(a, rm):
        full = jnp.concatenate([a] * (brows // 2), axis=0)
        return full * rm.reshape((brows,) + (1,) * (a.ndim - 1))

    def scatter_rows(zp):
        zp = jnp.swapaxes(zp.reshape(n_col // n_row, n_row, width, bcols * width), 0, 1)
        zp = zp.reshape(n_col * width, bcols * width)
        zr = lax.psum_scatter(zp, "row", scatter_dimension=0, tiled=True)
        return zr.reshape(n_col // n_row, width, bcols, width)

    f32 = jnp.float32
    member = [(supernode == s).astype(f32) for s in range(SUPERNODES)]
    struct = [
        jnp.logical_and(supernode > s, jnp.all(row_bits[:, s:] == 1, axis=1)).astype(f32)
        for s in range(SUPERNODES - 1)
    ]

    last = SUPERNODES - 1
    rM2, cM2 = rows_of(member[last]), cols_of(member[last])
    x = mask(pivot_inverse, rM2, cM2)

    S1, M1, S0, M0 = struct[1], member[1], struct[0], member[0]
    rS1, cS1, rM1, cM1 = rows_of(S1), cols_of(S1), rows_of(M1), cols_of(M1)
    rS0, cS0, rM0, cM0 = rows_of(S0), cols_of(S0), rows_of(M0), cols_of(M0)

    xm = mask(x, rS1, cS1)
    xc1 = pack_rows(xm.sum(axis=2))
    uc1 = pack_rows(mask(unit_factor, rS1, cM1).sum(axis=2))
    uc0 = mask(unit_factor, rS0, cM0).sum(axis=2)
    gcol = lax.all_gather(jnp.concatenate([xc1, uc1, uc0], axis=0), "col", axis=1)
    send = jnp.concatenate([uc1, uc0], axis=0)
    pieces = [send] + [lax.ppermute(send, "row", [(i, (i + d) % n_row) for i in range(n_row)]) for d in range(1, n_row)]
    by_shift = jnp.stack(pieces)
    grow = jnp.take(by_shift, (r - jnp.arange(n_row)) % n_row, axis=0)
    xg, urow1, urow0 = gcol[0:2], gcol[2:4], gcol[4:8]
    ucol1, ucol0 = grow[:, 0:2], grow[:, 2:6]

    s1 = S1.reshape(bcols, n_col).sum(axis=0)
    ueff = jnp.transpose(ucol1, (1, 0, 2, 3)).reshape(n_col, width, width) * s1[:, None, None]
    y = dot("pqax,qxb->pab", xg, ueff)
    yl = mask(unpack_rows(y, rS1)[:, :, None, :], None, cM1)
    x = x - yl
    wc = pack_rows(yl - xm)
    zp = dot("pqax,pacb->qxcb", urow1, wc)
    x = x + unpack_rows(scatter_rows(zp), rM1) + mask(pivot_inverse, rM1, cM1)

    xm = mask(x, rS0, cS0)
    xg = lax.all_gather(xm, "col", axis=2)
    u2 = ucol0.reshape(n_row, bcols, n_col // n_row, width, width)
    u2 = jnp.transpose(u2, (2, 0, 1, 3, 4)).reshape(n_col, bcols, width, width)
    y = dot("taqcx,qcxb->tab", xg, u2)
    yl = mask(y[:, :, None, :], None, cM0)
    x = x - yl
    zp = dot("tqax,tacb->qxcb", urow0, yl - xm)
    x = x + unpack_rows(scatter_rows(zp), rM0) + mask(pivot_inverse, rM0, cM0)
    return x


def solution(mesh):
    in_specs = (P(None, "row", None, "col"), P(None, "row", None, "col"), P(), P())
    out_specs = P(None, "row", None, "col")
    return jax.shard_map(shards, mesh=mesh, in_specs=in_specs, out_specs=out_specs, check_vma=False)
```

```python
import jax
import jax.numpy as jnp
from jax import lax
from jax.sharding import PartitionSpec as P

SUPERNODES = 3
PRECISION = lax.Precision.HIGH
COL_STAGES = ((1, 4), (4, 4))


def dot(spec, a, b):
    return jnp.einsum(spec, a, b, precision=PRECISION, preferred_element_type=jnp.float32)


def pp_gather(a, axis, stages):
    n = lax.axis_size(axis)
    me = lax.axis_index(axis)
    out = a[None]
    for stride, count in stages:
        def to(i, d, stride=stride, count=count):
            digit = (i // stride) % count
            return i + (((digit + d) % count) - digit) * stride

        parts = [out] + [lax.ppermute(out, axis, [(i, to(i, d)) for i in range(n)]) for d in range(1, count)]
        out = jnp.concatenate(parts, axis=0)
    src = jnp.arange(n)
    at = jnp.zeros((n,), jnp.int32)
    mult = 1
    for stride, count in stages:
        at = at + ((me // stride - src // stride) % count) * mult
        mult *= count
    return jnp.take(out, at, axis=0)


def shards(unit_factor, pivot_inverse, supernode, row_bits):
    n_row = lax.axis_size("row")
    n_col = lax.axis_size("col")
    brows, width, bcols, _ = unit_factor.shape
    nb = brows * n_row
    r = lax.axis_index("row")
    q = lax.axis_index("col")

    def rows_of(v):
        return lax.dynamic_index_in_dim(v.reshape(brows, n_row), r, axis=1, keepdims=False)

    def cols_of(v):
        return lax.dynamic_index_in_dim(v.reshape(bcols, n_col), q, axis=1, keepdims=False)

    def mask(a, rm=None, cm=None):
        if rm is not None:
            a = a * rm[:, None, None, None]
        if cm is not None:
            a = a * cm[None, None, :, None]
        return a

    def pack_rows(a):
        return a.reshape((brows // 2, 2) + a.shape[1:]).sum(axis=0)

    def unpack_rows(a, rm):
        full = jnp.concatenate([a] * (brows // 2), axis=0)
        return full * rm.reshape((brows,) + (1,) * (a.ndim - 1))

    def scatter_rows(zp):
        zp = jnp.swapaxes(zp.reshape(n_col // n_row, n_row, width, bcols * width), 0, 1)
        zp = zp.reshape(n_col * width, bcols * width)
        zr = lax.psum_scatter(zp, "row", scatter_dimension=0, tiled=True)
        return zr.reshape(n_col // n_row, width, bcols, width)

    f32 = jnp.float32
    member = [(supernode == s).astype(f32) for s in range(SUPERNODES)]
    struct = [
        jnp.logical_and(supernode > s, jnp.all(row_bits[:, s:] == 1, axis=1)).astype(f32)
        for s in range(SUPERNODES - 1)
    ]

    last = SUPERNODES - 1
    rM2, cM2 = rows_of(member[last]), cols_of(member[last])
    x = mask(pivot_inverse, rM2, cM2)

    S1, M1, S0, M0 = struct[1], member[1], struct[0], member[0]
    rS1, cS1, rM1, cM1 = rows_of(S1), cols_of(S1), rows_of(M1), cols_of(M1)
    rS0, cS0, rM0, cM0 = rows_of(S0), cols_of(S0), rows_of(M0), cols_of(M0)

    xm = mask(x, rS1, cS1)
    xc1 = pack_rows(xm.sum(axis=2))
    uc1 = pack_rows(mask(unit_factor, rS1, cM1).sum(axis=2))
    uc0 = mask(unit_factor, rS0, cM0).sum(axis=2)
    gcol = lax.all_gather(jnp.concatenate([xc1, uc1], axis=0), "col", axis=1)
    urow0 = pp_gather(uc0, "col", COL_STAGES)
    send = jnp.concatenate([uc1, uc0], axis=0)
    pieces = [send] + [lax.ppermute(send, "row", [(i, (i + d) % n_row) for i in range(n_row)]) for d in range(1, n_row)]
    by_shift = jnp.stack(pieces)
    grow = jnp.take(by_shift, (r - jnp.arange(n_row)) % n_row, axis=0)
    xg, urow1 = gcol[0:2], gcol[2:4]
    ucol1, ucol0 = grow[:, 0:2], grow[:, 2:6]

    s1 = S1.reshape(bcols, n_col).sum(axis=0)
    ueff = jnp.transpose(ucol1, (1, 0, 2, 3)).reshape(n_col, width, width) * s1[:, None, None]
    y = dot("pqax,qxb->pab", xg, ueff)
    yl = mask(unpack_rows(y, rS1)[:, :, None, :], None, cM1)
    x = x - yl
    wc = pack_rows(yl - xm)
    zp = dot("pqax,pacb->qxcb", urow1, wc)
    x = x + unpack_rows(scatter_rows(zp), rM1) + mask(pivot_inverse, rM1, cM1)

    xm = mask(x, rS0, cS0)
    xg = lax.all_gather(xm, "col", axis=2)
    u2 = ucol0.reshape(n_row, bcols, n_col // n_row, width, width)
    u2 = jnp.transpose(u2, (2, 0, 1, 3, 4)).reshape(n_col, bcols, width, width)
    y = dot("taqcx,qcxb->tab", xg, u2)
    yl = mask(y[:, :, None, :], None, cM0)
    x = x - yl
    zp = dot("qtax,tacb->qxcb", urow0, yl - xm)
    x = x + unpack_rows(scatter_rows(zp), rM0) + mask(pivot_inverse, rM0, cM0)
    return x


def solution(mesh):
    in_specs = (P(None, "row", None, "col"), P(None, "row", None, "col"), P(), P())
    out_specs = P(None, "row", None, "col")
    return jax.shard_map(shards, mesh=mesh, in_specs=in_specs, out_specs=out_specs, check_vma=False)
```

```python
import jax
import jax.numpy as jnp
from jax import lax
from jax.sharding import PartitionSpec as P


SUPERNODES = 3
PRECISION = lax.Precision.HIGH
COL_STAGES = ((1, 4), (4, 4))


def dot(spec, a, b):
    return jnp.einsum(spec, a, b, precision=PRECISION, preferred_element_type=jnp.float32)


def pp_gather(a, axis, stages):
    n = lax.axis_size(axis)
    me = lax.axis_index(axis)
    out = a[None]
    for stride, count in stages:
        def to(i, d, stride=stride, count=count):
            digit = (i // stride) % count
            return i + (((digit + d) % count) - digit) * stride

        parts = [out] + [lax.ppermute(out, axis, [(i, to(i, d)) for i in range(n)]) for d in range(1, count)]
        out = jnp.concatenate(parts, axis=0)
    src = jnp.arange(n)
    at = jnp.zeros((n,), jnp.int32)
    mult = 1
    for stride, count in stages:
        at = at + ((me // stride - src // stride) % count) * mult
        mult *= count
    return jnp.take(out, at, axis=0)


def shards(unit_factor, pivot_inverse, supernode, row_bits):
    n_row = lax.axis_size("row")
    n_col = lax.axis_size("col")
    brows, width, bcols, _ = unit_factor.shape
    r = lax.axis_index("row")
    q = lax.axis_index("col")

    def rows_of(v):
        return lax.dynamic_index_in_dim(v.reshape(brows, n_row), r, axis=1, keepdims=False)

    def cols_of(v):
        return lax.dynamic_index_in_dim(v.reshape(bcols, n_col), q, axis=1, keepdims=False)

    def mask(a, rm=None, cm=None):
        if rm is not None:
            a = a * rm[:, None, None, None]
        if cm is not None:
            a = a * cm[None, None, :, None]
        return a

    def pack_rows(a):
        return a.reshape((brows // 2, 2) + a.shape[1:]).sum(axis=0)

    def unpack_rows(a, rm):
        full = jnp.concatenate([a] * (brows // 2), axis=0)
        return full * rm.reshape((brows,) + (1,) * (a.ndim - 1))

    def scatter_rows(zp):
        zp = jnp.swapaxes(zp.reshape(n_col // n_row, n_row, width, bcols * width), 0, 1)
        zp = zp.reshape(n_col * width, bcols * width)
        zr = lax.psum_scatter(zp, "row", scatter_dimension=0, tiled=True)
        return zr.reshape(n_col // n_row, width, bcols, width)

    f32 = jnp.float32
    member = [(supernode == s).astype(f32) for s in range(SUPERNODES)]
    struct = [
        jnp.logical_and(supernode > s, jnp.all(row_bits[:, s:] == 1, axis=1)).astype(f32)
        for s in range(SUPERNODES - 1)
    ]

    last = SUPERNODES - 1
    rM2, cM2 = rows_of(member[last]), cols_of(member[last])
    x = mask(pivot_inverse, rM2, cM2)

    S1, M1, S0, M0 = struct[1], member[1], struct[0], member[0]
    rS1, cS1, rM1, cM1 = rows_of(S1), cols_of(S1), rows_of(M1), cols_of(M1)
    rS0, cS0, rM0, cM0 = rows_of(S0), cols_of(S0), rows_of(M0), cols_of(M0)

    xm = mask(x, rS1, cS1)
    xc1 = pack_rows(xm.sum(axis=2))
    uc1 = pack_rows(mask(unit_factor, rS1, cM1).sum(axis=2))
    uc0 = mask(unit_factor, rS0, cM0).sum(axis=2)
    xg = lax.all_gather(xc1, "col", axis=1)
    urow1 = pp_gather(uc1, "col", COL_STAGES)
    urow0 = pp_gather(uc0, "col", COL_STAGES)
    send = jnp.concatenate([uc1, uc0], axis=0)
    pieces = [send] + [lax.ppermute(send, "row", [(i, (i + d) % n_row) for i in range(n_row)]) for d in range(1, n_row)]
    by_shift = jnp.stack(pieces)
    grow = jnp.take(by_shift, (r - jnp.arange(n_row)) % n_row, axis=0)
    ucol1, ucol0 = grow[:, 0:2], grow[:, 2:6]

    s1 = S1.reshape(bcols, n_col).sum(axis=0)
    ueff = jnp.transpose(ucol1, (1, 0, 2, 3)).reshape(n_col, width, width) * s1[:, None, None]
    y = dot("pqax,qxb->pab", xg, ueff)
    yl = mask(unpack_rows(y, rS1)[:, :, None, :], None, cM1)
    x = x - yl
    wc = pack_rows(yl - xm)
    zp = dot("qpax,pacb->qxcb", urow1, wc)
    z1 = scatter_rows(zp)
    x = x + unpack_rows(z1, rM1) + mask(pivot_inverse, rM1, cM1)

    xm = mask(x, rS0, cS0)
    xg = lax.all_gather(xm, "col", axis=2)
    u2 = ucol0.reshape(n_row, bcols, n_col // n_row, width, width)
    u2 = jnp.transpose(u2, (2, 0, 1, 3, 4)).reshape(n_col, bcols, width, width)
    y = dot("taqcx,qcxb->tab", xg, u2)
    yl = mask(y[:, :, None, :], None, cM0)
    x = x - yl
    zp = dot("qtax,tacb->qxcb", urow0, yl - xm)
    x = x + unpack_rows(scatter_rows(zp), rM0) + mask(pivot_inverse, rM0, cM0)
    return x


def solution(mesh):
    in_specs = (P(None, "row", None, "col"), P(None, "row", None, "col"), P(), P())
    out_specs = P(None, "row", None, "col")
    return jax.shard_map(shards, mesh=mesh, in_specs=in_specs, out_specs=out_specs, check_vma=False)
```

```python
import jax
import jax.numpy as jnp
from jax import lax
from jax.sharding import PartitionSpec as P


SUPERNODES = 3
PRECISION = lax.Precision.HIGH
COL_STAGES = ((1, 4), (4, 4))


def dot(spec, a, b):
    return jnp.einsum(spec, a, b, precision=PRECISION, preferred_element_type=jnp.float32)


def pp_gather(a, axis, stages):
    n = lax.axis_size(axis)
    me = lax.axis_index(axis)
    out = a[None]
    for stride, count in stages:
        def to(i, d, stride=stride, count=count):
            digit = (i // stride) % count
            return i + (((digit + d) % count) - digit) * stride

        parts = [out] + [lax.ppermute(out, axis, [(i, to(i, d)) for i in range(n)]) for d in range(1, count)]
        out = jnp.concatenate(parts, axis=0)
    src = jnp.arange(n)
    at = jnp.zeros((n,), jnp.int32)
    mult = 1
    for stride, count in stages:
        at = at + ((me // stride - src // stride) % count) * mult
        mult *= count
    return jnp.take(out, at, axis=0)


def shards(unit_factor, pivot_inverse, supernode, row_bits):
    n_row = lax.axis_size("row")
    n_col = lax.axis_size("col")
    brows, width, bcols, _ = unit_factor.shape
    r = lax.axis_index("row")
    q = lax.axis_index("col")

    def rows_of(v):
        return lax.dynamic_index_in_dim(v.reshape(brows, n_row), r, axis=1, keepdims=False)

    def cols_of(v):
        return lax.dynamic_index_in_dim(v.reshape(bcols, n_col), q, axis=1, keepdims=False)

    def mask(a, rm=None, cm=None):
        if rm is not None:
            a = a * rm[:, None, None, None]
        if cm is not None:
            a = a * cm[None, None, :, None]
        return a

    def pack_rows(a):
        return a.reshape((brows // 2, 2) + a.shape[1:]).sum(axis=0)

    def unpack_rows(a, rm):
        full = jnp.concatenate([a] * (brows // 2), axis=0)
        return full * rm.reshape((brows,) + (1,) * (a.ndim - 1))

    def scatter_rows(zp):
        zp = jnp.swapaxes(zp.reshape(n_col // n_row, n_row, width, bcols * width), 0, 1)
        zp = zp.reshape(n_col * width, bcols * width)
        zr = lax.psum_scatter(zp, "row", scatter_dimension=0, tiled=True)
        return zr.reshape(n_col // n_row, width, bcols, width)

    f32 = jnp.float32
    member = [(supernode == s).astype(f32) for s in range(SUPERNODES)]
    struct = [
        jnp.logical_and(supernode > s, jnp.all(row_bits[:, s:] == 1, axis=1)).astype(f32)
        for s in range(SUPERNODES - 1)
    ]

    last = SUPERNODES - 1
    rM2, cM2 = rows_of(member[last]), cols_of(member[last])
    x = mask(pivot_inverse, rM2, cM2)

    S1, M1, S0, M0 = struct[1], member[1], struct[0], member[0]
    rS1, cS1, rM1, cM1 = rows_of(S1), cols_of(S1), rows_of(M1), cols_of(M1)
    rS0, cS0, rM0, cM0 = rows_of(S0), cols_of(S0), rows_of(M0), cols_of(M0)

    xm = mask(x, rS1, cS1)
    xc1 = pack_rows(xm.sum(axis=2))
    uc1 = pack_rows(mask(unit_factor, rS1, cM1).sum(axis=2))
    uc0 = mask(unit_factor, rS0, cM0).sum(axis=2)
    u1t = jnp.transpose(uc1, (2, 0, 1)).reshape(2, width, width)
    gcol = lax.all_gather(jnp.concatenate([xc1, u1t], axis=0), "col", axis=1)
    urow0 = pp_gather(uc0, "col", COL_STAGES)
    send = jnp.concatenate([uc1, uc0], axis=0)
    pieces = [send] + [lax.ppermute(send, "row", [(i, (i + d) % n_row) for i in range(n_row)]) for d in range(1, n_row)]
    by_shift = jnp.stack(pieces)
    grow = jnp.take(by_shift, (r - jnp.arange(n_row)) % n_row, axis=0)
    xg, urow1 = gcol[0:2], gcol[2:4]
    ucol1, ucol0 = grow[:, 0:2], grow[:, 2:6]

    s1 = S1.reshape(bcols, n_col).sum(axis=0)
    ueff = jnp.transpose(ucol1, (1, 0, 2, 3)).reshape(n_col, width, width) * s1[:, None, None]
    y = dot("pqax,qxb->pab", xg, ueff)
    yl = mask(unpack_rows(y, rS1)[:, :, None, :], None, cM1)
    x = x - yl
    wc = pack_rows(yl - xm)
    u1m = jnp.transpose(urow1, (1, 0, 2, 3)).reshape(n_col * width, 2 * width)
    zp = dot("ij,jk->ik", u1m, wc.reshape(2 * width, bcols * width)).reshape(n_col, width, bcols, width)
    z1 = scatter_rows(zp)
    x = x + unpack_rows(z1, rM1) + mask(pivot_inverse, rM1, cM1)

    xm = mask(x, rS0, cS0)
    xg = lax.all_gather(xm, "col", axis=2)
    u2 = ucol0.reshape(n_row, bcols, n_col // n_row, width, width)
    u2 = jnp.transpose(u2, (2, 0, 1, 3, 4)).reshape(n_col, bcols, width, width)
    y = dot("taqcx,qcxb->tab", xg, u2)
    yl = mask(y[:, :, None, :], None, cM0)
    x = x - yl
    zp = dot("qtax,tacb->qxcb", urow0, yl - xm)
    x = x + unpack_rows(scatter_rows(zp), rM0) + mask(pivot_inverse, rM0, cM0)
    return x


def solution(mesh):
    in_specs = (P(None, "row", None, "col"), P(None, "row", None, "col"), P(), P())
    out_specs = P(None, "row", None, "col")
    return jax.shard_map(shards, mesh=mesh, in_specs=in_specs, out_specs=out_specs, check_vma=False)
```

```python
import jax
import jax.numpy as jnp
from jax import lax
from jax.sharding import PartitionSpec as P


SUPERNODES = 3
PRECISION = lax.Precision.HIGH
COL_STAGES = ((1, 4), (4, 4))


def dot(spec, a, b):
    return jnp.einsum(spec, a, b, precision=PRECISION, preferred_element_type=jnp.float32)


def pp_gather(a, axis, stages):
    n = lax.axis_size(axis)
    me = lax.axis_index(axis)
    out = a[None]
    for stride, count in stages:
        def to(i, d, stride=stride, count=count):
            digit = (i // stride) % count
            return i + (((digit + d) % count) - digit) * stride

        parts = [out] + [lax.ppermute(out, axis, [(i, to(i, d)) for i in range(n)]) for d in range(1, count)]
        out = jnp.concatenate(parts, axis=0)
    src = jnp.arange(n)
    at = jnp.zeros((n,), jnp.int32)
    mult = 1
    for stride, count in stages:
        at = at + ((me // stride - src // stride) % count) * mult
        mult *= count
    return jnp.take(out, at, axis=0)


def shards(unit_factor, pivot_inverse, supernode, row_bits):
    n_row = lax.axis_size("row")
    n_col = lax.axis_size("col")
    brows, width, bcols, _ = unit_factor.shape
    r = lax.axis_index("row")
    q = lax.axis_index("col")

    def rows_of(v):
        return lax.dynamic_index_in_dim(v.reshape(brows, n_row), r, axis=1, keepdims=False)

    def cols_of(v):
        return lax.dynamic_index_in_dim(v.reshape(bcols, n_col), q, axis=1, keepdims=False)

    def mask(a, rm=None, cm=None):
        if rm is not None:
            a = a * rm[:, None, None, None]
        if cm is not None:
            a = a * cm[None, None, :, None]
        return a

    def pack_rows(a):
        return a.reshape((brows // 2, 2) + a.shape[1:]).sum(axis=0)

    def unpack_rows(a, rm):
        full = jnp.concatenate([a] * (brows // 2), axis=0)
        return full * rm.reshape((brows,) + (1,) * (a.ndim - 1))

    def scatter_rows(zp):
        zp = jnp.swapaxes(zp.reshape(n_col // n_row, n_row, width, bcols * width), 0, 1)
        zp = zp.reshape(n_col * width, bcols * width)
        zr = lax.psum_scatter(zp, "row", scatter_dimension=0, tiled=True)
        return zr.reshape(n_col // n_row, width, bcols, width)

    f32 = jnp.float32
    member = [(supernode == s).astype(f32) for s in range(SUPERNODES)]
    struct = [
        jnp.logical_and(supernode > s, jnp.all(row_bits[:, s:] == 1, axis=1)).astype(f32)
        for s in range(SUPERNODES - 1)
    ]

    last = SUPERNODES - 1
    rM2, cM2 = rows_of(member[last]), cols_of(member[last])
    x = mask(pivot_inverse, rM2, cM2)

    S1, M1, S0, M0 = struct[1], member[1], struct[0], member[0]
    rS1, cS1, rM1, cM1 = rows_of(S1), cols_of(S1), rows_of(M1), cols_of(M1)
    rS0, cS0, rM0, cM0 = rows_of(S0), cols_of(S0), rows_of(M0), cols_of(M0)

    xm = mask(x, rS1, cS1)
    xc1 = pack_rows(xm.sum(axis=2))
    uc1 = pack_rows(mask(unit_factor, rS1, cM1).sum(axis=2))
    uc0 = mask(unit_factor, rS0, cM0).sum(axis=2)
    gcol = lax.all_gather(jnp.concatenate([xc1, uc1], axis=0), "col", axis=1)
    urow0 = pp_gather(uc0, "col", COL_STAGES)
    send = jnp.concatenate([uc1, uc0], axis=0)
    pieces = [send] + [lax.ppermute(send, "row", [(i, (i + d) % n_row) for i in range(n_row)]) for d in range(1, n_row)]
    by_shift = jnp.stack(pieces)
    grow = jnp.take(by_shift, (r - jnp.arange(n_row)) % n_row, axis=0)
    xg, urow1 = gcol[0:2], gcol[2:4]
    ucol1, ucol0 = grow[:, 0:2], grow[:, 2:6]

    s1 = S1.reshape(bcols, n_col).sum(axis=0)
    ueff = jnp.transpose(ucol1, (1, 0, 2, 3)).reshape(n_col, width, width) * s1[:, None, None]
    y = dot("pqax,qxb->pab", xg, ueff)
    yl = mask(unpack_rows(y, rS1)[:, :, None, :], None, cM1)
    x = x - yl
    wc = pack_rows(yl - xm)
    zp = dot("pqax,pacb->qxcb", urow1, wc)
    z1 = scatter_rows(zp)
    x = x + unpack_rows(z1, rM1) + mask(pivot_inverse, rM1, cM1)

    xm = mask(x, rS0, cS0)
    xg = lax.all_gather(xm, "col", axis=2)
    u2 = ucol0.reshape(n_row, bcols, n_col // n_row, width, width)
    u2 = jnp.transpose(u2, (2, 0, 1, 3, 4)).reshape(n_col, bcols, width, width)
    y = dot("taqcx,qcxb->tab", xg, u2)
    yl = mask(y[:, :, None, :], None, cM0)
    x = x - yl + mask(pivot_inverse, rM0, cM0)
    zp = dot("qtax,tacb->qxcb", urow0, yl - xm)
    return x + unpack_rows(scatter_rows(zp), rM0)


def solution(mesh):
    in_specs = (P(None, "row", None, "col"), P(None, "row", None, "col"), P(), P())
    out_specs = P(None, "row", None, "col")
    return jax.shard_map(shards, mesh=mesh, in_specs=in_specs, out_specs=out_specs, check_vma=False)
```

```python
import jax
import jax.numpy as jnp
from jax import lax
from jax.sharding import PartitionSpec as P


SUPERNODES = 3
PRECISION = lax.Precision.HIGH
COL_STAGES = ((1, 4), (4, 4))


def dot(spec, a, b):
    return jnp.einsum(spec, a, b, precision=PRECISION, preferred_element_type=jnp.float32)


def pp_gather(a, axis, stages):
    n = lax.axis_size(axis)
    me = lax.axis_index(axis)
    out = a[None]
    for stride, count in stages:
        def to(i, d, stride=stride, count=count):
            digit = (i // stride) % count
            return i + (((digit + d) % count) - digit) * stride

        parts = [out] + [lax.ppermute(out, axis, [(i, to(i, d)) for i in range(n)]) for d in range(1, count)]
        out = jnp.concatenate(parts, axis=0)
    src = jnp.arange(n)
    at = jnp.zeros((n,), jnp.int32)
    mult = 1
    for stride, count in stages:
        at = at + ((me // stride - src // stride) % count) * mult
        mult *= count
    return jnp.take(out, at, axis=0)


def shards(unit_factor, pivot_inverse, supernode, row_bits):
    n_row = lax.axis_size("row")
    n_col = lax.axis_size("col")
    brows, width, bcols, _ = unit_factor.shape
    r = lax.axis_index("row")
    q = lax.axis_index("col")

    def rows_of(v):
        return lax.dynamic_index_in_dim(v.reshape(brows, n_row), r, axis=1, keepdims=False)

    def cols_of(v):
        return lax.dynamic_index_in_dim(v.reshape(bcols, n_col), q, axis=1, keepdims=False)

    def mask(a, rm=None, cm=None):
        if rm is not None:
            a = a * rm[:, None, None, None]
        if cm is not None:
            a = a * cm[None, None, :, None]
        return a

    def pack_rows(a):
        return a.reshape((brows // 2, 2) + a.shape[1:]).sum(axis=0)

    def unpack_rows(a, rm):
        full = jnp.concatenate([a] * (brows // 2), axis=0)
        return full * rm.reshape((brows,) + (1,) * (a.ndim - 1))

    def scatter_rows(zp):
        zp = jnp.swapaxes(zp.reshape(n_col // n_row, n_row, width, bcols * width), 0, 1)
        zp = zp.reshape(n_col * width, bcols * width)
        zr = lax.psum_scatter(zp, "row", scatter_dimension=0, tiled=True)
        return zr.reshape(n_col // n_row, width, bcols, width)

    f32 = jnp.float32
    member = [(supernode == s).astype(f32) for s in range(SUPERNODES)]
    struct = [
        jnp.logical_and(supernode > s, jnp.all(row_bits[:, s:] == 1, axis=1)).astype(f32)
        for s in range(SUPERNODES - 1)
    ]

    last = SUPERNODES - 1
    rM2, cM2 = rows_of(member[last]), cols_of(member[last])
    x = mask(pivot_inverse, rM2, cM2)

    S1, M1, S0, M0 = struct[1], member[1], struct[0], member[0]
    rS1, cS1, rM1, cM1 = rows_of(S1), cols_of(S1), rows_of(M1), cols_of(M1)
    rS0, cS0, rM0, cM0 = rows_of(S0), cols_of(S0), rows_of(M0), cols_of(M0)

    xm = mask(x, rS1, cS1)
    xc1 = pack_rows(xm.sum(axis=2))
    uc1 = pack_rows(mask(unit_factor, rS1, cM1).sum(axis=2))
    uc0 = mask(unit_factor, rS0, cM0).sum(axis=2)
    gcol = lax.all_gather(jnp.concatenate([xc1, uc1], axis=0), "col", axis=1)
    urow0 = pp_gather(uc0, "col", COL_STAGES)
    send = jnp.concatenate([uc1, uc0], axis=0)
    pieces = [send] + [lax.ppermute(send, "row", [(i, (i + d) % n_row) for i in range(n_row)]) for d in range(1, n_row)]
    by_shift = jnp.stack(pieces)
    grow = jnp.take(by_shift, (r - jnp.arange(n_row)) % n_row, axis=0)
    xg, urow1 = gcol[0:2], gcol[2:4]
    ucol1, ucol0 = grow[:, 0:2], grow[:, 2:6]

    s1 = S1.reshape(bcols, n_col).sum(axis=0)
    ueff = jnp.transpose(ucol1, (1, 0, 2, 3)).reshape(n_col, width, width) * s1[:, None, None]
    y = dot("pqax,qxb->pab", xg, ueff)
    yl = mask(unpack_rows(y, rS1)[:, :, None, :], None, cM1)
    wc = pack_rows(yl - xm)
    x = x - yl + mask(pivot_inverse, rM1, cM1)
    zp = dot("pqax,pacb->qxcb", urow1, wc)
    z1 = scatter_rows(zp)
    x = x + unpack_rows(z1, rM1)

    xm = mask(x, rS0, cS0)
    xg = lax.all_gather(xm, "col", axis=2)
    u2 = ucol0.reshape(n_row, bcols, n_col // n_row, width, width)
    u2 = jnp.transpose(u2, (2, 0, 1, 3, 4)).reshape(n_col, bcols, width, width)
    y = dot("taqcx,qcxb->tab", xg, u2)
    yl = mask(y[:, :, None, :], None, cM0)
    x = x - yl
    zp = dot("qtax,tacb->qxcb", urow0, yl - xm)
    x = x + unpack_rows(scatter_rows(zp), rM0) + mask(pivot_inverse, rM0, cM0)
    return x


def solution(mesh):
    in_specs = (P(None, "row", None, "col"), P(None, "row", None, "col"), P(), P())
    out_specs = P(None, "row", None, "col")
    return jax.shard_map(shards, mesh=mesh, in_specs=in_specs, out_specs=out_specs, check_vma=False)
```
